128 devices in a mesh: row: 8 (over z, core), col: 16 (over x, y).
Axes of the slice: x: 4, y: 4, z: 4, core: 2. Of those that a mesh axis runs over, the one named last changes fastest.
Arguments:
- recorded: bfloat16 [2048, 64, 3072], P(('row', 'col')), may hold values from -6 to 6
- seg_count: int32 [128], P(('row', 'col')), may hold values from 0 to 16, as said below
- slot_station: int32 [2048], P(('row', 'col')), may hold values from 0 to 1023, as said below
- window_mask: int32 [1024, 64], P(('row', 'col')), may hold values from 0 to 1, as said below
Outputs:
- cross_real: bfloat16 [1024, 1024, 384], P('row', 'col')
- cross_imag: bfloat16 [1024, 1024, 384], P('row', 'col')
The draws below stay inside these ranges and needn't reach their ends.
Inputs may be any that keep to these rules, and one draw needn't show every extreme that they name: `seg_count`: recorder d = r * 16 + c serves row r of the grid; in every row exactly half of the 16 recorders have 16 live slots and the others none. `slot_station`: the live slots of the recorders of row r name each station of r * 128 to (r + 1) * 128 - 1 exactly once; a recorder's live slots name 2 or no stations of each owner (stations with equal s // 8); dead slots name arbitrary stations. `window_mask`: A station's invalid windows form one cyclic run of 0 to 64 windows.
All inputs are finite; a program needn't handle non-finite values.
Results may differ from the reference program's by a relative error of at most 0.0066.
Values may be sent and summed in bfloat16 or wider, within the bound.
No kernel may reach another device: no remote copies, remote signals or barrier semaphores. Data moves between devices by JAX's collectives and lax.ppermute only.
A program may use at most 128 MiB of HBM per device.

```python
import math
import jax
import jax.numpy as jnp
from jax import lax

F = 384
L = 3072
F0 = 13
BAND = 64
S_DEV = 8
W = 64
RECS = 16
GRID_ROWS = 8
R_ST = 16
S_ROW = 128
NCB = 64
S = 1024
SLOTS = 2048


def recorder_layout(key):
    half = RECS // 2
    pairs = S_DEV // 2

    def one_row(row):
        row_key = jax.random.fold_in(jax.random.fold_in(key, 7001), row)
        busy = jax.random.permutation(jax.random.fold_in(row_key, 1), RECS).astype(jnp.int32)
        owner_keys = jax.random.split(jax.random.fold_in(row_key, 2), RECS)
        orders = jax.vmap(lambda k: jax.random.permutation(k, S_DEV))(owner_keys).astype(jnp.int32)
        owners = jnp.arange(RECS, dtype=jnp.int32)
        which = jnp.arange(half, dtype=jnp.int32)
        offset = (which[:, None] - owners[None, :]) % half
        usable = offset < pairs
        first = jnp.minimum(2 * offset, S_DEV - 2)
        owner_grid = jnp.broadcast_to(owners[None, :], (half, RECS))
        station_a = orders[owner_grid, first]
        station_b = orders[owner_grid, first + 1]
        base = row * S_ROW + owner_grid * S_DEV
        entries = jnp.stack([base + station_a, base + station_b], axis=2).reshape(half, 2 * RECS)
        valid = jnp.stack([usable, usable], axis=2).reshape(half, 2 * RECS)
        position = jnp.arange(2 * RECS, dtype=jnp.int32)
        sort_key = jnp.where(valid, position[None, :], 2 * RECS + position[None, :])
        picked = jnp.argsort(sort_key, axis=1, stable=True)[:, :R_ST]
        lists = jnp.take_along_axis(entries, picked, axis=1)
        shuffle_keys = jax.random.split(jax.random.fold_in(row_key, 3), half)
        shuffles = jax.vmap(lambda k: jax.random.permutation(k, R_ST))(shuffle_keys)
        lists = jnp.take_along_axis(lists, shuffles, axis=1)
        filler = jax.random.randint(jax.random.fold_in(row_key, 4), (RECS, R_ST), 0, S, dtype=jnp.int32)
        table = filler.at[busy[:half]].set(lists)
        counts = jnp.zeros((RECS,), jnp.int32).at[busy[:half]].set(R_ST)
        return (table.reshape(RECS * R_ST), counts)
    tables, counts = jax.vmap(one_row)(jnp.arange(GRID_ROWS, dtype=jnp.int32))
    return (tables.reshape(SLOTS).astype(jnp.int32), counts.reshape(RECS * GRID_ROWS).astype(jnp.int32))


def draw_seg_count(key, part):
    return recorder_layout(key)[1]


def draw_slot_station(key, part):
    return recorder_layout(key)[0]


def draw_window_mask(key, part):
    start = jax.random.randint(jax.random.fold_in(key, 11), (S, 1), 0, W, dtype=jnp.int32)
    length = jax.random.randint(jax.random.fold_in(key, 12), (S, 1), 0, W + 1, dtype=jnp.int32)
    windows = jnp.arange(W, dtype=jnp.int32)[None, :]
    outage = (windows - start) % W < length
    return jnp.where(outage, 0, 1).astype(jnp.int32)


def steps_of(rng, dims, cuts, low, largest):
    gain, own = 1.0, jax.random.fold_in(rng, 6)
    for dim, parts in cuts:
        steps = jnp.exp(jax.random.uniform(jax.random.fold_in(own, dim), (parts,), jnp.float32, low / len(cuts), largest / len(cuts)))
        gain = gain * jnp.repeat(steps, dims[dim] // parts).reshape([-1 if axis == dim else 1 for axis in range(len(dims))])
    return gain


def normal_values(own_key, dims, spread, most, cuts=(), kind=jnp.bfloat16):
    result = spread * jax.random.normal(own_key, dims, jnp.float32)
    if cuts:
        result = result * steps_of(own_key, dims, cuts, -0.22, 0.18)
    return jnp.clip(result, -most, most).astype(kind)


def setup_inputs(seed: int = 0) -> dict:
    seeds = jax.random.split(jax.random.key(seed), 5)
    recorded = normal_values(seeds[0], (SLOTS, W, L), 1.0, 6.0, ((0, 128),))
    seg_count = draw_seg_count(jax.random.fold_in(seeds[4], 71), 0)
    slot_station = draw_slot_station(jax.random.fold_in(seeds[4], 71), 0)
    window_mask = draw_window_mask(jax.random.fold_in(seeds[4], 71), 0)
    return dict(recorded=recorded, seg_count=seg_count, slot_station=slot_station, window_mask=window_mask)


def transform_table():
    times = jnp.arange(L, dtype=jnp.int32)
    freqs = jnp.arange(F, dtype=jnp.int32) + F0
    phase = times[:, None] * freqs[None, :] % L
    angle = phase.astype(jnp.float32) * (2.0 * math.pi / L)
    return jnp.concatenate([jnp.cos(angle), -jnp.sin(angle)], axis=1).astype(jnp.bfloat16)

def whiten(segments, table):
    count = segments.shape[0]
    spectrum = jnp.dot(segments.reshape(count * W, L), table, preferred_element_type=jnp.float32)
    real = spectrum[:, :F]
    imag = spectrum[:, F:]
    power = (real * real + imag * imag).reshape(count * W, F // BAND, BAND)
    factor = lax.rsqrt(lax.optimization_barrier(jnp.mean(power, axis=2)) + 1e-05)
    factor = jnp.repeat(factor, BAND, axis=1)
    white = jnp.concatenate([real * factor, imag * factor], axis=1)
    return white.astype(jnp.bfloat16).reshape(count, W, 2 * F)

def reference(recorded, seg_count, slot_station, window_mask):
    table = transform_table()
    slot = jnp.arange(SLOTS, dtype=jnp.int32)
    live = slot % R_ST < seg_count[slot // R_ST]
    target = jnp.where(live, slot_station, S).astype(jnp.int32)
    source = jnp.zeros((S,), jnp.int32).at[target].set(slot, mode='drop')
    blocks = source.reshape(S // S_DEV, S_DEV)

    def one_block(index):
        return whiten(jnp.take(recorded, index, axis=0), table)
    spectra = lax.map(one_block, blocks).reshape(S, W, 2 * F)
    mask_float = window_mask.astype(jnp.bfloat16)
    spectra = spectra * mask_float[:, :, None]
    stacked = spectra.reshape(S, W, 2, F).transpose(3, 0, 2, 1).reshape(F, S, 2 * W)
    column = jnp.arange(S, dtype=jnp.int32)
    within = column % NCB
    order = ((within // S_DEV * RECS + column // NCB) * S_DEV + within % S_DEV).astype(jnp.int32)
    right = jnp.take(stacked, order, axis=1)
    right_mask = jnp.take(mask_float, order, axis=0)
    counts = jnp.dot(mask_float, right_mask.T, preferred_element_type=jnp.float32)
    inverse = 1.0 / jnp.maximum(counts, 1.0)
    swapped = jnp.concatenate([right[:, :, W:], -right[:, :, :W]], axis=2)

    def one_bin(group):
        left, plain, turned = group
        left = left.astype(jnp.float32)
        real = jnp.dot(left, plain.astype(jnp.float32).T)
        imag = jnp.dot(left, turned.astype(jnp.float32).T)
        return ((real * inverse).astype(jnp.bfloat16), (imag * inverse).astype(jnp.bfloat16))
    cross_real, cross_imag = lax.map(one_bin, (stacked, right, swapped))
    return (cross_real.transpose(1, 2, 0), cross_imag.transpose(1, 2, 0))
```

```python
import math

import jax
import jax.numpy as jnp
from jax import lax
from jax.sharding import PartitionSpec as P

F = 384
L = 3072
F0 = 13
BAND = 64
CAP = 2
W = 64


def transform_table():
    freqs = jnp.arange(F, dtype=jnp.int32) + F0
    high = jnp.arange(L // 64, dtype=jnp.int32)[:, None] * 64 * freqs[None, :] % L
    low = jnp.arange(64, dtype=jnp.int32)[:, None] * freqs[None, :] % L
    scale = 2.0 * math.pi / L
    ah = high.astype(jnp.float32) * scale
    al = low.astype(jnp.float32) * scale
    ch, sh = jnp.cos(ah)[:, None, :], jnp.sin(ah)[:, None, :]
    cl, sl = jnp.cos(al)[None, :, :], jnp.sin(al)[None, :, :]
    cos_part = (ch * cl - sh * sl).reshape(L, F)
    sin_part = (sh * cl + ch * sl).reshape(L, F)
    return jnp.concatenate([cos_part, -sin_part], axis=1).astype(jnp.bfloat16)


def whiten(segments, table):
    count = segments.shape[0]
    spectrum = jnp.dot(segments.reshape(count * W, L), table, preferred_element_type=jnp.float32)
    real = spectrum[:, :F]
    imag = spectrum[:, F:]
    power = (real * real + imag * imag).reshape(count * W, F // BAND, BAND)
    factor = lax.rsqrt(jnp.mean(power, axis=2) + 1e-05)
    factor = jnp.repeat(factor, BAND, axis=1)
    white = jnp.concatenate([real * factor, imag * factor], axis=1)
    return white.astype(jnp.bfloat16).reshape(count, W, 2 * F)


def per_device(recorded, seg_count, slot_station, window_mask):
    columns = lax.axis_size("col")
    slots_here = recorded.shape[0]
    owned = window_mask.shape[0]
    outgoing = columns * CAP
    slot_index = jnp.arange(slots_here, dtype=jnp.int32)
    live = slot_index < seg_count[0]
    target_col = jnp.where(live, slot_station // owned % columns, columns)
    onehot = (target_col[:, None] == jnp.arange(columns, dtype=jnp.int32)[None, :]).astype(
        jnp.int32
    )
    earlier = jnp.cumsum(onehot, axis=0) - onehot
    rank = jnp.sum(earlier * onehot, axis=1)
    position = jnp.where(live, target_col * CAP + rank, outgoing)
    chosen = position[None, :] == jnp.arange(outgoing, dtype=jnp.int32)[:, None]
    source = jnp.sum(jnp.where(chosen, slot_index[None, :], 0), axis=1)
    local_id = jnp.sum(jnp.where(chosen, slot_station[None, :] % owned + 1, 0), axis=1) - 1
    labels = local_id.astype(jnp.bfloat16).reshape(columns, CAP)
    table = transform_table()
    local_white = whiten(recorded, table)
    payload = jnp.take(local_white, source, axis=0).reshape(columns, CAP, W, 2 * F)
    arrived, tags = (
        lax.all_to_all(payload, "col", split_axis=0, concat_axis=0, tiled=True),
        lax.all_to_all(labels, "col", split_axis=0, concat_axis=0, tiled=True),
    )
    tags = tags.reshape(outgoing).astype(jnp.int32)
    flat = arrived.reshape(outgoing, W, arrived.shape[3])
    match = tags[None, :] == jnp.arange(owned, dtype=jnp.int32)[:, None]
    pick = jnp.sum(jnp.where(match, jnp.arange(outgoing, dtype=jnp.int32)[None, :], 0), axis=1)
    spectra = jnp.take(flat, pick, axis=0)
    mask_float = window_mask.astype(jnp.bfloat16)
    spectra = spectra * mask_float[:, :, None]
    stacked = spectra.reshape(owned, W, 2, F).transpose(3, 0, 2, 1).reshape(F, owned, 2 * W)
    left, left_mask = (
        lax.all_gather(stacked, "col", axis=1, tiled=True),
        lax.all_gather(mask_float, "col", axis=0, tiled=True),
    )
    right, right_mask = (
        lax.all_gather(stacked, "row", axis=1, tiled=True),
        lax.all_gather(mask_float, "row", axis=0, tiled=True),
    )
    counts = jnp.dot(left_mask, right_mask.T, preferred_element_type=jnp.float32)
    inverse = 1.0 / jnp.maximum(counts, 1.0)
    across = right.shape[1]
    turned = jnp.concatenate([right[:, :, W:], -right[:, :, :W]], axis=2)
    both = jnp.concatenate([right, turned], axis=1)
    product = jnp.einsum("fiw,fjw->ijf", left, both, preferred_element_type=jnp.float32)
    real_part = (product[:, :across, :] * inverse[:, :, None]).astype(jnp.bfloat16)
    imag_part = (product[:, across:, :] * inverse[:, :, None]).astype(jnp.bfloat16)
    return (real_part, imag_part)


def solution(mesh):
    placed = (
        P(("row", "col"), None, None),
        P(("row", "col")),
        P(("row", "col")),
        P(("row", "col"), None),
    )
    return jax.shard_map(
        per_device,
        mesh=mesh,
        in_specs=placed,
        out_specs=(P("row", "col", None), P("row", "col", None)),
        check_vma=False,
    )
```

```python
import math

import jax
import jax.numpy as jnp
from jax import lax
from jax.sharding import PartitionSpec as P

F = 384
L = 3072
F0 = 13
BAND = 64
CAP = 2
W = 64


def transform_table():
    freqs = jnp.arange(F, dtype=jnp.int32) + F0
    high = jnp.arange(L // 64, dtype=jnp.int32)[:, None] * 64 * freqs[None, :] % L
    low = jnp.arange(64, dtype=jnp.int32)[:, None] * freqs[None, :] % L
    scale = 2.0 * math.pi / L
    ah = high.astype(jnp.float32) * scale
    al = low.astype(jnp.float32) * scale
    ch, sh = jnp.cos(ah)[:, None, :], jnp.sin(ah)[:, None, :]
    cl, sl = jnp.cos(al)[None, :, :], jnp.sin(al)[None, :, :]
    cos_part = (ch * cl - sh * sl).reshape(L, F)
    sin_part = (sh * cl + ch * sl).reshape(L, F)
    return jnp.concatenate([cos_part, -sin_part], axis=1).astype(jnp.bfloat16)


def whiten(segments, table):
    count = segments.shape[0]
    spectrum = jnp.dot(segments.reshape(count * W, L), table, preferred_element_type=jnp.float32)
    real = spectrum[:, :F]
    imag = spectrum[:, F:]
    power = (real * real + imag * imag).reshape(count * W, F // BAND, BAND)
    factor = lax.rsqrt(jnp.mean(power, axis=2) + 1e-05)
    factor = jnp.repeat(factor, BAND, axis=1)
    white = jnp.concatenate([real * factor, imag * factor], axis=1)
    return white.astype(jnp.bfloat16).reshape(count, W, 2 * F)


def per_device(recorded, seg_count, slot_station, window_mask):
    columns = lax.axis_size("col")
    slots_here = recorded.shape[0]
    owned = window_mask.shape[0]
    outgoing = columns * CAP
    slot_index = jnp.arange(slots_here, dtype=jnp.int32)
    live = slot_index < seg_count[0]
    target_col = jnp.where(live, slot_station // owned % columns, columns)
    onehot = (target_col[:, None] == jnp.arange(columns, dtype=jnp.int32)[None, :]).astype(
        jnp.int32
    )
    earlier = jnp.cumsum(onehot, axis=0) - onehot
    rank = jnp.sum(earlier * onehot, axis=1)
    position = jnp.where(live, target_col * CAP + rank, outgoing)
    chosen = position[None, :] == jnp.arange(outgoing, dtype=jnp.int32)[:, None]
    source = jnp.sum(jnp.where(chosen, slot_index[None, :], 0), axis=1)
    local_id = jnp.sum(jnp.where(chosen, slot_station[None, :] % owned + 1, 0), axis=1) - 1
    labels = local_id.astype(jnp.bfloat16).reshape(columns, CAP)
    table = transform_table()
    local_white = whiten(recorded, table)
    payload = jnp.take(local_white, source, axis=0).reshape(columns, CAP * W, 2 * F)
    label_rows = jnp.zeros((columns, 8, 2 * F), jnp.bfloat16).at[:, 0, :CAP].set(labels)
    payload = jnp.concatenate([payload, label_rows], axis=1)
    arrived = lax.all_to_all(payload, "col", split_axis=0, concat_axis=0, tiled=True)
    tags = arrived[:, CAP * W, :CAP].reshape(outgoing).astype(jnp.int32)
    flat = arrived[:, : CAP * W, :].reshape(outgoing, W, 2 * F)
    match = tags[None, :] == jnp.arange(owned, dtype=jnp.int32)[:, None]
    pick = jnp.sum(jnp.where(match, jnp.arange(outgoing, dtype=jnp.int32)[None, :], 0), axis=1)
    spectra = jnp.take(flat, pick, axis=0)
    mask_float = window_mask.astype(jnp.bfloat16)
    spectra = spectra * mask_float[:, :, None]
    stacked = spectra.reshape(owned, W, 2, F).transpose(3, 0, 2, 1).reshape(F, owned, 2 * W)
    mask_row = jnp.concatenate([mask_float, jnp.zeros_like(mask_float)], axis=1)
    stacked = jnp.concatenate([stacked, mask_row[None]], axis=0)
    left_all = lax.all_gather(stacked, "col", axis=1, tiled=True)
    right_all = lax.all_gather(stacked, "row", axis=1, tiled=True)
    left, left_mask = left_all[:F], left_all[F, :, :W]
    right, right_mask = right_all[:F], right_all[F, :, :W]
    counts = jnp.dot(left_mask, right_mask.T, preferred_element_type=jnp.float32)
    inverse = 1.0 / jnp.maximum(counts, 1.0)
    lane = jnp.arange(2 * W, dtype=jnp.int32)
    swap = jnp.where(
        lane[:, None] == (lane[None, :] + W) % (2 * W),
        jnp.where(lane[None, :] < W, 1.0, -1.0),
        0.0,
    ).astype(jnp.bfloat16)
    turned = jnp.einsum("fjw,wv->fjv", right, swap, preferred_element_type=jnp.float32).astype(
        jnp.bfloat16
    )
    real = jnp.einsum("fiw,fjw->ijf", left, right, preferred_element_type=jnp.float32)
    imag = jnp.einsum("fiw,fjw->ijf", left, turned, preferred_element_type=jnp.float32)
    real_part = (real * inverse[:, :, None]).astype(jnp.bfloat16)
    imag_part = (imag * inverse[:, :, None]).astype(jnp.bfloat16)
    return (real_part, imag_part)


def solution(mesh):
    placed = (
        P(("row", "col"), None, None),
        P(("row", "col")),
        P(("row", "col")),
        P(("row", "col"), None),
    )
    return jax.shard_map(
        per_device,
        mesh=mesh,
        in_specs=placed,
        out_specs=(P("row", "col", None), P("row", "col", None)),
        check_vma=False,
    )
```

```python
import math

import jax
import jax.numpy as jnp
from jax import lax
from jax.sharding import PartitionSpec as P

F = 384
L = 3072
F0 = 13
BAND = 64
CAP = 2
CHUNKS = 3
W = 64


def transform_table(first, count):
    freqs = jnp.arange(count, dtype=jnp.int32) + (F0 + first)
    high = jnp.arange(L // 64, dtype=jnp.int32)[:, None] * 64 * freqs[None, :] % L
    low = jnp.arange(64, dtype=jnp.int32)[:, None] * freqs[None, :] % L
    scale = 2.0 * math.pi / L
    ah = high.astype(jnp.float32) * scale
    al = low.astype(jnp.float32) * scale
    ch, sh = jnp.cos(ah)[:, None, :], jnp.sin(ah)[:, None, :]
    cl, sl = jnp.cos(al)[None, :, :], jnp.sin(al)[None, :, :]
    cos_part = (ch * cl - sh * sl).reshape(L, count)
    sin_part = (sh * cl + ch * sl).reshape(L, count)
    return jnp.concatenate([cos_part, -sin_part], axis=1).astype(jnp.bfloat16)


def whiten(segments, table):
    count = segments.shape[0]
    width = table.shape[1] // 2
    spectrum = jnp.dot(segments.reshape(count * W, L), table, preferred_element_type=jnp.float32)
    real = spectrum[:, :width]
    imag = spectrum[:, width:]
    power = (real * real + imag * imag).reshape(count * W, width // BAND, BAND)
    factor = lax.rsqrt(jnp.mean(power, axis=2) + 1e-05)
    factor = jnp.repeat(factor, BAND, axis=1)
    white = jnp.concatenate([real * factor, imag * factor], axis=1)
    return white.astype(jnp.bfloat16).reshape(count, W, 2 * width)


def per_device(recorded, seg_count, slot_station, window_mask):
    columns = lax.axis_size("col")
    slots_here = recorded.shape[0]
    owned = window_mask.shape[0]
    outgoing = columns * CAP
    slot_index = jnp.arange(slots_here, dtype=jnp.int32)
    live = slot_index < seg_count[0]
    target_col = jnp.where(live, slot_station // owned % columns, columns)
    onehot = (target_col[:, None] == jnp.arange(columns, dtype=jnp.int32)[None, :]).astype(
        jnp.int32
    )
    earlier = jnp.cumsum(onehot, axis=0) - onehot
    rank = jnp.sum(earlier * onehot, axis=1)
    position = jnp.where(live, target_col * CAP + rank, outgoing)
    chosen = position[None, :] == jnp.arange(outgoing, dtype=jnp.int32)[:, None]
    source = jnp.sum(jnp.where(chosen, slot_index[None, :], 0), axis=1)
    local_id = jnp.sum(jnp.where(chosen, slot_station[None, :] % owned + 1, 0), axis=1) - 1
    labels = local_id.astype(jnp.bfloat16).reshape(columns, CAP)
    mask_float = window_mask.astype(jnp.bfloat16)
    lane = jnp.arange(2 * W, dtype=jnp.int32)
    swap = jnp.where(
        lane[:, None] == (lane[None, :] + W) % (2 * W),
        jnp.where(lane[None, :] < W, 1.0, -1.0),
        0.0,
    ).astype(jnp.bfloat16)
    chunk = F // CHUNKS
    pick = inverse = None
    reals, imags = [], []
    for k in range(CHUNKS):
        table = transform_table(k * chunk, chunk)
        local_white = whiten(recorded, table)
        payload = jnp.take(local_white, source, axis=0).reshape(columns, CAP * W, 2 * chunk)
        if k == 0:
            label_rows = jnp.zeros((columns, 8, 2 * chunk), jnp.bfloat16).at[:, 0, :CAP].set(labels)
            payload = jnp.concatenate([payload, label_rows], axis=1)
        arrived = lax.all_to_all(payload, "col", split_axis=0, concat_axis=0, tiled=True)
        if k == 0:
            tags = arrived[:, CAP * W, :CAP].reshape(outgoing).astype(jnp.int32)
            match = tags[None, :] == jnp.arange(owned, dtype=jnp.int32)[:, None]
            pick = jnp.sum(
                jnp.where(match, jnp.arange(outgoing, dtype=jnp.int32)[None, :], 0), axis=1
            )
        flat = arrived[:, : CAP * W, :].reshape(outgoing, W, 2 * chunk)
        spectra = jnp.take(flat, pick, axis=0) * mask_float[:, :, None]
        stacked = spectra.reshape(owned, W, 2, chunk).transpose(3, 0, 2, 1)
        stacked = stacked.reshape(chunk, owned, 2 * W)
        if k == 0:
            mask_row = jnp.concatenate([mask_float, jnp.zeros_like(mask_float)], axis=1)
            stacked = jnp.concatenate([stacked, mask_row[None]], axis=0)
        left = lax.all_gather(stacked, "col", axis=1, tiled=True)
        right = lax.all_gather(stacked, "row", axis=1, tiled=True)
        if k == 0:
            left_mask, right_mask = left[chunk, :, :W], right[chunk, :, :W]
            left, right = left[:chunk], right[:chunk]
            counts = jnp.dot(left_mask, right_mask.T, preferred_element_type=jnp.float32)
            inverse = 1.0 / jnp.maximum(counts, 1.0)
        turned = jnp.einsum(
            "fjw,wv->fjv", right, swap, preferred_element_type=jnp.float32
        ).astype(jnp.bfloat16)
        real = jnp.einsum("fiw,fjw->ijf", left, right, preferred_element_type=jnp.float32)
        imag = jnp.einsum("fiw,fjw->ijf", left, turned, preferred_element_type=jnp.float32)
        reals.append((real * inverse[:, :, None]).astype(jnp.bfloat16))
        imags.append((imag * inverse[:, :, None]).astype(jnp.bfloat16))
    return (jnp.concatenate(reals, axis=2), jnp.concatenate(imags, axis=2))


def solution(mesh):
    placed = (
        P(("row", "col"), None, None),
        P(("row", "col")),
        P(("row", "col")),
        P(("row", "col"), None),
    )
    return jax.shard_map(
        per_device,
        mesh=mesh,
        in_specs=placed,
        out_specs=(P("row", "col", None), P("row", "col", None)),
        check_vma=False,
    )
```

```python
import math

import jax
import jax.numpy as jnp
from jax import lax
from jax.sharding import PartitionSpec as P

F = 384
L = 3072
F0 = 13
BAND = 64
CAP = 2
W = 64


def transform_table():
    freqs = jnp.arange(F, dtype=jnp.int32) + F0
    high = jnp.arange(L // 64, dtype=jnp.int32)[:, None] * 64 * freqs[None, :] % L
    low = jnp.arange(64, dtype=jnp.int32)[:, None] * freqs[None, :] % L
    scale = 2.0 * math.pi / L
    ah = high.astype(jnp.float32) * scale
    al = low.astype(jnp.float32) * scale
    ch, sh = jnp.cos(ah)[:, None, :], jnp.sin(ah)[:, None, :]
    cl, sl = jnp.cos(al)[None, :, :], jnp.sin(al)[None, :, :]
    cos_part = (ch * cl - sh * sl).reshape(L, F)
    sin_part = (sh * cl + ch * sl).reshape(L, F)
    return jnp.concatenate([cos_part, -sin_part], axis=1).astype(jnp.bfloat16)


def whiten(segments, table):
    count = segments.shape[0]
    spectrum = jnp.dot(segments.reshape(count * W, L), table, preferred_element_type=jnp.float32)
    real = spectrum[:, :F]
    imag = spectrum[:, F:]
    power = (real * real + imag * imag).reshape(count * W, F // BAND, BAND)
    factor = lax.rsqrt(jnp.mean(power, axis=2) + 1e-05)
    factor = jnp.repeat(factor, BAND, axis=1)
    white = jnp.concatenate([real * factor, imag * factor], axis=1)
    return white.astype(jnp.bfloat16).reshape(count, W, 2 * F)


def per_device(recorded, seg_count, slot_station, window_mask):
    columns = lax.axis_size("col")
    slots_here = recorded.shape[0]
    owned = window_mask.shape[0]
    outgoing = columns * CAP
    slot_index = jnp.arange(slots_here, dtype=jnp.int32)
    live = slot_index < seg_count[0]
    target_col = jnp.where(live, slot_station // owned % columns, columns)
    onehot = (target_col[:, None] == jnp.arange(columns, dtype=jnp.int32)[None, :]).astype(
        jnp.int32
    )
    earlier = jnp.cumsum(onehot, axis=0) - onehot
    rank = jnp.sum(earlier * onehot, axis=1)
    position = jnp.where(live, target_col * CAP + rank, outgoing)
    chosen = position[None, :] == jnp.arange(outgoing, dtype=jnp.int32)[:, None]
    source = jnp.sum(jnp.where(chosen, slot_index[None, :], 0), axis=1)
    local_id = jnp.sum(jnp.where(chosen, slot_station[None, :] % owned + 1, 0), axis=1) - 1
    labels = local_id.astype(jnp.bfloat16).reshape(columns, CAP)
    table = transform_table()
    local_white = whiten(recorded, table)
    payload = jnp.take(local_white, source, axis=0).reshape(columns, CAP * W, 2 * F)
    label_rows = jnp.zeros((columns, 8, 2 * F), jnp.bfloat16).at[:, 0, :CAP].set(labels)
    payload = jnp.concatenate([payload, label_rows], axis=1)
    arrived = lax.all_to_all(payload, "col", split_axis=0, concat_axis=0, tiled=True)
    tags = arrived[:, CAP * W, :CAP].reshape(outgoing).astype(jnp.int32)
    flat = arrived[:, : CAP * W, :].reshape(outgoing, W, 2 * F)
    match = tags[None, :] == jnp.arange(owned, dtype=jnp.int32)[:, None]
    pick = jnp.sum(jnp.where(match, jnp.arange(outgoing, dtype=jnp.int32)[None, :], 0), axis=1)
    spectra = jnp.take(flat, pick, axis=0)
    mask_float = window_mask.astype(jnp.bfloat16)
    spectra = spectra * mask_float[:, :, None]
    stacked = spectra.reshape(owned, W, 2, F).transpose(3, 0, 2, 1).reshape(F, owned, 2 * W)
    mask_row = jnp.concatenate([mask_float, jnp.zeros_like(mask_float)], axis=1)
    stacked = jnp.concatenate([stacked, mask_row[None]], axis=0)
    left_all = lax.all_gather(stacked, "col", axis=1, tiled=True)
    rows = lax.axis_size("row")
    copies = jnp.broadcast_to(stacked[None], (rows,) + stacked.shape)
    got = lax.all_to_all(copies, "row", split_axis=0, concat_axis=0, tiled=True)
    right_all = got.transpose(1, 0, 2, 3).reshape(F + 1, rows * owned, 2 * W)
    left, left_mask = left_all[:F], left_all[F, :, :W]
    right, right_mask = right_all[:F], right_all[F, :, :W]
    counts = jnp.dot(left_mask, right_mask.T, preferred_element_type=jnp.float32)
    inverse = 1.0 / jnp.maximum(counts, 1.0)
    lane = jnp.arange(2 * W, dtype=jnp.int32)
    swap = jnp.where(
        lane[:, None] == (lane[None, :] + W) % (2 * W),
        jnp.where(lane[None, :] < W, 1.0, -1.0),
        0.0,
    ).astype(jnp.bfloat16)
    turned = jnp.einsum("fjw,wv->fjv", right, swap, preferred_element_type=jnp.float32).astype(
        jnp.bfloat16
    )
    real = jnp.einsum("fiw,fjw->ijf", left, right, preferred_element_type=jnp.float32)
    imag = jnp.einsum("fiw,fjw->ijf", left, turned, preferred_element_type=jnp.float32)
    real_part = (real * inverse[:, :, None]).astype(jnp.bfloat16)
    imag_part = (imag * inverse[:, :, None]).astype(jnp.bfloat16)
    return (real_part, imag_part)


def solution(mesh):
    placed = (
        P(("row", "col"), None, None),
        P(("row", "col")),
        P(("row", "col")),
        P(("row", "col"), None),
    )
    return jax.shard_map(
        per_device,
        mesh=mesh,
        in_specs=placed,
        out_specs=(P("row", "col", None), P("row", "col", None)),
        check_vma=False,
    )
```

```python
import math

import jax
import jax.numpy as jnp
from jax import lax
from jax.sharding import PartitionSpec as P

F = 384
L = 3072
F0 = 13
BAND = 64
CAP = 2
SC_ROWS = 232
W = 64


def transform_table():
    freqs = jnp.arange(F, dtype=jnp.int32) + F0
    high = jnp.arange(L // 64, dtype=jnp.int32)[:, None] * 64 * freqs[None, :] % L
    low = jnp.arange(64, dtype=jnp.int32)[:, None] * freqs[None, :] % L
    scale = 2.0 * math.pi / L
    ah = high.astype(jnp.float32) * scale
    al = low.astype(jnp.float32) * scale
    ch, sh = jnp.cos(ah)[:, None, :], jnp.sin(ah)[:, None, :]
    cl, sl = jnp.cos(al)[None, :, :], jnp.sin(al)[None, :, :]
    cos_part = (ch * cl - sh * sl).reshape(L, F)
    sin_part = (sh * cl + ch * sl).reshape(L, F)
    return jnp.concatenate([cos_part, -sin_part], axis=1).astype(jnp.bfloat16)


def whiten(segments, table):
    count = segments.shape[0]
    spectrum = jnp.dot(segments.reshape(count * W, L), table, preferred_element_type=jnp.float32)
    real = spectrum[:, :F]
    imag = spectrum[:, F:]
    power = (real * real + imag * imag).reshape(count * W, F // BAND, BAND)
    factor = lax.rsqrt(jnp.mean(power, axis=2) + 1e-05)
    factor = jnp.repeat(factor, BAND, axis=1)
    white = jnp.concatenate([real * factor, imag * factor], axis=1)
    return white.astype(jnp.bfloat16).reshape(count, W, 2 * F)


def per_device(recorded, seg_count, slot_station, window_mask):
    columns = lax.axis_size("col")
    slots_here = recorded.shape[0]
    owned = window_mask.shape[0]
    outgoing = columns * CAP
    slot_index = jnp.arange(slots_here, dtype=jnp.int32)
    live = slot_index < seg_count[0]
    target_col = jnp.where(live, slot_station // owned % columns, columns)
    onehot = (target_col[:, None] == jnp.arange(columns, dtype=jnp.int32)[None, :]).astype(
        jnp.int32
    )
    earlier = jnp.cumsum(onehot, axis=0) - onehot
    rank = jnp.sum(earlier * onehot, axis=1)
    position = jnp.where(live, target_col * CAP + rank, outgoing)
    chosen = position[None, :] == jnp.arange(outgoing, dtype=jnp.int32)[:, None]
    source = jnp.sum(jnp.where(chosen, slot_index[None, :], 0), axis=1)
    local_id = jnp.sum(jnp.where(chosen, slot_station[None, :] % owned + 1, 0), axis=1) - 1
    labels = local_id.astype(jnp.bfloat16).reshape(columns, CAP)
    table = transform_table()
    local_white = whiten(recorded, table)
    payload = jnp.take(local_white, source, axis=0).reshape(columns, CAP * W, 2 * F)
    label_rows = jnp.zeros((columns, 8, 2 * F), jnp.bfloat16).at[:, 0, :CAP].set(labels)
    payload = jnp.concatenate([payload, label_rows], axis=1)
    arrived = lax.all_to_all(payload, "col", split_axis=0, concat_axis=0, tiled=True)
    tags = arrived[:, CAP * W, :CAP].reshape(outgoing).astype(jnp.int32)
    flat = arrived[:, : CAP * W, :].reshape(outgoing, W, 2 * F)
    match = tags[None, :] == jnp.arange(owned, dtype=jnp.int32)[:, None]
    pick = jnp.sum(jnp.where(match, jnp.arange(outgoing, dtype=jnp.int32)[None, :], 0), axis=1)
    spectra = jnp.take(flat, pick, axis=0)
    mask_float = window_mask.astype(jnp.bfloat16)
    spectra = spectra * mask_float[:, :, None]
    stacked = spectra.reshape(owned, W, 2, F).transpose(3, 0, 2, 1).reshape(F, owned, 2 * W)
    mask_row = jnp.concatenate([mask_float, jnp.zeros_like(mask_float)], axis=1)
    stacked = jnp.concatenate([stacked, mask_row[None]], axis=0)
    split = SC_ROWS
    sc_left = lax.all_gather(stacked[:split], "col", axis=1, tiled=True)
    tc_copies = jnp.broadcast_to(stacked[None, split:], (columns,) + stacked[split:].shape)
    tc_got = lax.all_to_all(tc_copies, "col", split_axis=0, concat_axis=0, tiled=True)
    tc_left = tc_got.transpose(1, 0, 2, 3).reshape(F + 1 - split, columns * owned, 2 * W)
    left_all = jnp.concatenate([sc_left, tc_left], axis=0)
    rows = lax.axis_size("row")
    here = lax.axis_index("row")
    got = jnp.broadcast_to(stacked[None], (rows,) + stacked.shape)
    for shift in range(1, rows):
        moved = lax.ppermute(stacked, "row", [(s, (s + shift) % rows) for s in range(rows)])
        got = lax.dynamic_update_index_in_dim(got, moved, (here - shift) % rows, 0)
    right_all = got.transpose(1, 0, 2, 3).reshape(F + 1, rows * owned, 2 * W)
    left, left_mask = left_all[:F], left_all[F, :, :W]
    right, right_mask = right_all[:F], right_all[F, :, :W]
    counts = jnp.dot(left_mask, right_mask.T, preferred_element_type=jnp.float32)
    inverse = 1.0 / jnp.maximum(counts, 1.0)
    lane = jnp.arange(2 * W, dtype=jnp.int32)
    swap = jnp.where(
        lane[:, None] == (lane[None, :] + W) % (2 * W),
        jnp.where(lane[None, :] < W, 1.0, -1.0),
        0.0,
    ).astype(jnp.bfloat16)
    turned = jnp.einsum("fjw,wv->fjv", right, swap, preferred_element_type=jnp.float32).astype(
        jnp.bfloat16
    )
    real = jnp.einsum("fiw,fjw->ijf", left, right, preferred_element_type=jnp.float32)
    imag = jnp.einsum("fiw,fjw->ijf", left, turned, preferred_element_type=jnp.float32)
    real_part = (real * inverse[:, :, None]).astype(jnp.bfloat16)
    imag_part = (imag * inverse[:, :, None]).astype(jnp.bfloat16)
    return (real_part, imag_part)


def solution(mesh):
    placed = (
        P(("row", "col"), None, None),
        P(("row", "col")),
        P(("row", "col")),
        P(("row", "col"), None),
    )
    return jax.shard_map(
        per_device,
        mesh=mesh,
        in_specs=placed,
        out_specs=(P("row", "col", None), P("row", "col", None)),
        check_vma=False,
    )
```

```python
import math

import jax
import jax.numpy as jnp
from jax import lax
from jax.sharding import PartitionSpec as P

F = 384
L = 3072
F0 = 13
BAND = 64
CAP = 2
W = 64


def transform_table():
    freqs = jnp.arange(F, dtype=jnp.int32) + F0
    high = jnp.arange(L // 64, dtype=jnp.int32)[:, None] * 64 * freqs[None, :] % L
    low = jnp.arange(64, dtype=jnp.int32)[:, None] * freqs[None, :] % L
    scale = 2.0 * math.pi / L
    ah = high.astype(jnp.float32) * scale
    al = low.astype(jnp.float32) * scale
    ch, sh = jnp.cos(ah)[:, None, :], jnp.sin(ah)[:, None, :]
    cl, sl = jnp.cos(al)[None, :, :], jnp.sin(al)[None, :, :]
    cos_part = (ch * cl - sh * sl).reshape(L, F)
    sin_part = (sh * cl + ch * sl).reshape(L, F)
    return jnp.concatenate([cos_part, -sin_part], axis=1).astype(jnp.bfloat16)


def whiten(segments, table):
    count = segments.shape[0]
    spectrum = jnp.dot(segments.reshape(count * W, L), table, preferred_element_type=jnp.float32)
    real = spectrum[:, :F]
    imag = spectrum[:, F:]
    power = (real * real + imag * imag).reshape(count * W, F // BAND, BAND)
    factor = lax.rsqrt(jnp.mean(power, axis=2) + 1e-05)
    factor = jnp.repeat(factor, BAND, axis=1)
    white = jnp.concatenate([real * factor, imag * factor], axis=1)
    return white.astype(jnp.bfloat16).reshape(count, W, 2 * F)


def per_device(recorded, seg_count, slot_station, window_mask):
    columns = lax.axis_size("col")
    slots_here = recorded.shape[0]
    owned = window_mask.shape[0]
    outgoing = columns * CAP
    slot_index = jnp.arange(slots_here, dtype=jnp.int32)
    live = slot_index < seg_count[0]
    target_col = jnp.where(live, slot_station // owned % columns, columns)
    onehot = (target_col[:, None] == jnp.arange(columns, dtype=jnp.int32)[None, :]).astype(
        jnp.int32
    )
    earlier = jnp.cumsum(onehot, axis=0) - onehot
    rank = jnp.sum(earlier * onehot, axis=1)
    position = jnp.where(live, target_col * CAP + rank, outgoing)
    chosen = position[None, :] == jnp.arange(outgoing, dtype=jnp.int32)[:, None]
    source = jnp.sum(jnp.where(chosen, slot_index[None, :], 0), axis=1)
    local_id = jnp.sum(jnp.where(chosen, slot_station[None, :] % owned + 1, 0), axis=1) - 1
    labels = local_id.astype(jnp.bfloat16).reshape(columns, CAP)
    table = transform_table()
    local_white = whiten(recorded, table)
    payload = jnp.take(local_white, source, axis=0).reshape(columns, CAP * W, 2 * F)
    label_rows = jnp.zeros((columns, 8, 2 * F), jnp.bfloat16).at[:, 0, :CAP].set(labels)
    payload = jnp.concatenate([payload, label_rows], axis=1)
    arrived = lax.all_to_all(payload, "col", split_axis=0, concat_axis=0, tiled=True)
    tags = arrived[:, CAP * W, :CAP].reshape(outgoing).astype(jnp.int32)
    flat = arrived[:, : CAP * W, :].reshape(outgoing, W, 2 * F)
    match = tags[None, :] == jnp.arange(owned, dtype=jnp.int32)[:, None]
    pick = jnp.sum(jnp.where(match, jnp.arange(outgoing, dtype=jnp.int32)[None, :], 0), axis=1)
    spectra = jnp.take(flat, pick, axis=0)
    mask_float = window_mask.astype(jnp.bfloat16)
    spectra = spectra * mask_float[:, :, None]
    stacked = spectra.reshape(owned, W, 2, F).transpose(3, 0, 2, 1).reshape(F, owned, 2 * W)
    mask_row = jnp.concatenate([mask_float, jnp.zeros_like(mask_float)], axis=1)
    stacked = jnp.concatenate([stacked, mask_row[None]], axis=0)
    left_all = lax.all_gather(stacked, "col", axis=1, tiled=True)
    rows = lax.axis_size("row")
    copies = jnp.broadcast_to(stacked[None], (rows,) + stacked.shape)
    got = lax.all_to_all(copies, "row", split_axis=0, concat_axis=0, tiled=True)
    right_all = got.transpose(1, 0, 2, 3).reshape(F + 1, rows * owned, 2 * W)
    left, left_mask = left_all[:F], left_all[F, :, :W]
    right, right_mask = right_all[:F], right_all[F, :, :W]
    counts = jnp.dot(left_mask, right_mask.T, preferred_element_type=jnp.float32)
    inverse = 1.0 / jnp.maximum(counts, 1.0)
    lane = jnp.arange(2 * W, dtype=jnp.int32)
    swap = jnp.where(
        lane[:, None] == (lane[None, :] + W) % (2 * W),
        jnp.where(lane[None, :] < W, 1.0, -1.0),
        0.0,
    ).astype(jnp.bfloat16)
    turned = jnp.einsum("fjw,wv->fjv", right, swap, preferred_element_type=jnp.float32).astype(
        jnp.bfloat16
    )
    across = right.shape[1]
    both = jnp.concatenate([right, turned], axis=1)
    product = jnp.einsum("fiw,fjw->ijf", left, both, preferred_element_type=jnp.float32)
    scaled = (product * jnp.concatenate([inverse, inverse], axis=1)[:, :, None]).astype(jnp.bfloat16)
    return (scaled[:, :across], scaled[:, across:])


def solution(mesh):
    placed = (
        P(("row", "col"), None, None),
        P(("row", "col")),
        P(("row", "col")),
        P(("row", "col"), None),
    )
    return jax.shard_map(
        per_device,
        mesh=mesh,
        in_specs=placed,
        out_specs=(P("row", "col", None), P("row", "col", None)),
        check_vma=False,
    )
```

```python
import math

import jax
import jax.numpy as jnp
from jax import lax
from jax.experimental import pallas as pl
from jax.experimental.pallas import tpu as pltpu
from jax.sharding import PartitionSpec as P

F = 384
L = 3072
F0 = 13
BAND = 64
CAP = 2
W = 64


FB = 128

def cross_kernel(l_ref, r_ref, inv_ref, re_ref, im_ref, acc_ref):
    ni = l_ref.shape[1]
    nj = r_ref.shape[1]
    half = r_ref.shape[2] // 2
    lane = lax.broadcasted_iota(jnp.int32, (nj, 2 * half), 1)
    sign = jnp.where(lane < half, 1.0, -1.0).astype(jnp.float32)

    def per_f(f, carry):
        rf = r_ref[f]
        tf = (pltpu.roll(rf.astype(jnp.float32), half, 1) * sign).astype(rf.dtype)
        both = jnp.concatenate([rf, tf], axis=0)
        res = lax.dot_general(l_ref[f], both, (((1,), (1,)), ((), ())),
                              preferred_element_type=jnp.float32)
        acc_ref[pl.ds(pl.multiple_of(f * ni, ni), ni), :] = res
        return carry

    lax.fori_loop(0, FB, per_f, 0)

    def per_i(i, carry):
        x = acc_ref[pl.ds(i, FB, stride=ni), :]
        y = (x * inv_ref[pl.ds(i, 1), :]).T
        re_ref[i] = y[:nj].astype(re_ref.dtype)
        im_ref[i] = y[nj:].astype(im_ref.dtype)
        return carry

    lax.fori_loop(0, ni, per_i, 0)


def cross(left, right, inverse2, nf):
    ni, nj, w2 = left.shape[1], right.shape[1], left.shape[2]
    out = jax.ShapeDtypeStruct((ni, nj, nf), jnp.bfloat16)
    return pl.pallas_call(
        cross_kernel,
        grid=(nf // FB,),
        in_specs=[
            pl.BlockSpec((FB, ni, w2), lambda f: (f, 0, 0)),
            pl.BlockSpec((FB, nj, w2), lambda f: (f, 0, 0)),
            pl.BlockSpec((ni, 2 * nj), lambda f: (0, 0)),
        ],
        out_specs=[
            pl.BlockSpec((ni, nj, FB), lambda f: (0, 0, f)),
            pl.BlockSpec((ni, nj, FB), lambda f: (0, 0, f)),
        ],
        out_shape=[out, out],
        scratch_shapes=[pltpu.VMEM((FB * ni, 2 * nj), jnp.float32)],
    )(left, right, inverse2)


def transform_table():
    freqs = jnp.arange(F, dtype=jnp.int32) + F0
    high = jnp.arange(L // 64, dtype=jnp.int32)[:, None] * 64 * freqs[None, :] % L
    low = jnp.arange(64, dtype=jnp.int32)[:, None] * freqs[None, :] % L
    scale = 2.0 * math.pi / L
    ah = high.astype(jnp.float32) * scale
    al = low.astype(jnp.float32) * scale
    ch, sh = jnp.cos(ah)[:, None, :], jnp.sin(ah)[:, None, :]
    cl, sl = jnp.cos(al)[None, :, :], jnp.sin(al)[None, :, :]
    cos_part = (ch * cl - sh * sl).reshape(L, F)
    sin_part = (sh * cl + ch * sl).reshape(L, F)
    return jnp.concatenate([cos_part, -sin_part], axis=1).astype(jnp.bfloat16)


def whiten(segments, table):
    count = segments.shape[0]
    spectrum = jnp.dot(segments.reshape(count * W, L), table, preferred_element_type=jnp.float32)
    real = spectrum[:, :F]
    imag = spectrum[:, F:]
    power = (real * real + imag * imag).reshape(count * W, F // BAND, BAND)
    factor = lax.rsqrt(jnp.mean(power, axis=2) + 1e-05)
    factor = jnp.repeat(factor, BAND, axis=1)
    white = jnp.concatenate([real * factor, imag * factor], axis=1)
    return white.astype(jnp.bfloat16).reshape(count, W, 2 * F)


def per_device(recorded, seg_count, slot_station, window_mask):
    columns = lax.axis_size("col")
    slots_here = recorded.shape[0]
    owned = window_mask.shape[0]
    outgoing = columns * CAP
    slot_index = jnp.arange(slots_here, dtype=jnp.int32)
    live = slot_index < seg_count[0]
    target_col = jnp.where(live, slot_station // owned % columns, columns)
    onehot = (target_col[:, None] == jnp.arange(columns, dtype=jnp.int32)[None, :]).astype(
        jnp.int32
    )
    earlier = jnp.cumsum(onehot, axis=0) - onehot
    rank = jnp.sum(earlier * onehot, axis=1)
    position = jnp.where(live, target_col * CAP + rank, outgoing)
    chosen = position[None, :] == jnp.arange(outgoing, dtype=jnp.int32)[:, None]
    source = jnp.sum(jnp.where(chosen, slot_index[None, :], 0), axis=1)
    local_id = jnp.sum(jnp.where(chosen, slot_station[None, :] % owned + 1, 0), axis=1) - 1
    labels = local_id.astype(jnp.bfloat16).reshape(columns, CAP)
    table = transform_table()
    local_white = whiten(recorded, table)
    payload = jnp.take(local_white, source, axis=0).reshape(columns, CAP * W, 2 * F)
    label_rows = jnp.zeros((columns, 8, 2 * F), jnp.bfloat16).at[:, 0, :CAP].set(labels)
    payload = jnp.concatenate([payload, label_rows], axis=1)
    arrived = lax.all_to_all(payload, "col", split_axis=0, concat_axis=0, tiled=True)
    tags = arrived[:, CAP * W, :CAP].reshape(outgoing).astype(jnp.int32)
    flat = arrived[:, : CAP * W, :].reshape(outgoing, W, 2 * F)
    match = tags[None, :] == jnp.arange(owned, dtype=jnp.int32)[:, None]
    pick = jnp.sum(jnp.where(match, jnp.arange(outgoing, dtype=jnp.int32)[None, :], 0), axis=1)
    spectra = jnp.take(flat, pick, axis=0)
    mask_float = window_mask.astype(jnp.bfloat16)
    spectra = spectra * mask_float[:, :, None]
    stacked = spectra.reshape(owned, W, 2, F).transpose(3, 0, 2, 1).reshape(F, owned, 2 * W)
    mask_row = jnp.concatenate([mask_float, jnp.zeros_like(mask_float)], axis=1)
    stacked = jnp.concatenate([stacked, mask_row[None]], axis=0)
    left_all = lax.all_gather(stacked, "col", axis=1, tiled=True)
    rows = lax.axis_size("row")
    copies = jnp.broadcast_to(stacked[None], (rows,) + stacked.shape)
    got = lax.all_to_all(copies, "row", split_axis=0, concat_axis=0, tiled=True)
    right_all = got.transpose(1, 0, 2, 3).reshape(F + 1, rows * owned, 2 * W)
    left_mask = left_all[F, :, :W]
    right_mask = right_all[F, :, :W]
    counts = jnp.dot(left_mask, right_mask.T, preferred_element_type=jnp.float32)
    inverse = 1.0 / jnp.maximum(counts, 1.0)
    return tuple(cross(left_all, right_all, jnp.concatenate([inverse, inverse], axis=1), F))


def solution(mesh):
    placed = (
        P(("row", "col"), None, None),
        P(("row", "col")),
        P(("row", "col")),
        P(("row", "col"), None),
    )
    return jax.shard_map(
        per_device,
        mesh=mesh,
        in_specs=placed,
        out_specs=(P("row", "col", None), P("row", "col", None)),
        check_vma=False,
    )
```

```python
import math

import jax
import jax.numpy as jnp
from jax import lax
from jax.sharding import PartitionSpec as P

F = 384
L = 3072
F0 = 13
BAND = 64
CAP = 2
W = 64


def transform_table():
    freqs = jnp.arange(F, dtype=jnp.int32) + F0
    high = jnp.arange(L // 64, dtype=jnp.int32)[:, None] * 64 * freqs[None, :] % L
    low = jnp.arange(64, dtype=jnp.int32)[:, None] * freqs[None, :] % L
    scale = 2.0 * math.pi / L
    ah = high.astype(jnp.float32) * scale
    al = low.astype(jnp.float32) * scale
    ch, sh = jnp.cos(ah)[:, None, :], jnp.sin(ah)[:, None, :]
    cl, sl = jnp.cos(al)[None, :, :], jnp.sin(al)[None, :, :]
    cos_part = (ch * cl - sh * sl).reshape(L, F)
    sin_part = (sh * cl + ch * sl).reshape(L, F)
    return jnp.concatenate([cos_part, -sin_part], axis=1).astype(jnp.bfloat16)


def whiten(segments, table):
    count = segments.shape[0]
    spectrum = jnp.dot(segments.reshape(count * W, L), table, preferred_element_type=jnp.float32)
    real = spectrum[:, :F]
    imag = spectrum[:, F:]
    power = (real * real + imag * imag).reshape(count * W, F // BAND, BAND)
    factor = lax.rsqrt(jnp.mean(power, axis=2) + 1e-05)
    factor = jnp.repeat(factor, BAND, axis=1)
    white = jnp.concatenate([real * factor, imag * factor], axis=1)
    return white.astype(jnp.bfloat16).reshape(count, W, 2 * F)


def per_device(recorded, seg_count, slot_station, window_mask):
    columns = lax.axis_size("col")
    slots_here = recorded.shape[0]
    owned = window_mask.shape[0]
    outgoing = columns * CAP
    slot_index = jnp.arange(slots_here, dtype=jnp.int32)
    live = slot_index < seg_count[0]
    target_col = jnp.where(live, slot_station // owned % columns, columns)
    onehot = (target_col[:, None] == jnp.arange(columns, dtype=jnp.int32)[None, :]).astype(
        jnp.int32
    )
    earlier = jnp.cumsum(onehot, axis=0) - onehot
    rank = jnp.sum(earlier * onehot, axis=1)
    position = jnp.where(live, target_col * CAP + rank, outgoing)
    chosen = position[None, :] == jnp.arange(outgoing, dtype=jnp.int32)[:, None]
    source = jnp.sum(jnp.where(chosen, slot_index[None, :], 0), axis=1)
    local_id = jnp.sum(jnp.where(chosen, slot_station[None, :] % owned + 1, 0), axis=1) - 1
    labels = local_id.astype(jnp.bfloat16).reshape(columns, CAP)
    table = transform_table()
    local_white = whiten(recorded, table)
    payload = jnp.take(local_white, source, axis=0).reshape(columns, CAP * W, 2 * F)
    label_rows = jnp.zeros((columns, 8, 2 * F), jnp.bfloat16).at[:, 0, :CAP].set(labels)
    payload = jnp.concatenate([payload, label_rows], axis=1)
    arrived = lax.all_to_all(payload, "col", split_axis=0, concat_axis=0, tiled=True)
    tags = arrived[:, CAP * W, :CAP].reshape(outgoing).astype(jnp.int32)
    flat = arrived[:, : CAP * W, :].reshape(outgoing, W, 2 * F)
    match = tags[None, :] == jnp.arange(owned, dtype=jnp.int32)[:, None]
    pick = jnp.sum(jnp.where(match, jnp.arange(outgoing, dtype=jnp.int32)[None, :], 0), axis=1)
    spectra = jnp.take(flat, pick, axis=0)
    mask_float = window_mask.astype(jnp.bfloat16)
    spectra = spectra * mask_float[:, :, None]
    stacked = spectra.reshape(owned, W, 2, F).transpose(3, 0, 2, 1).reshape(F, owned, 2 * W)
    mask_row = jnp.concatenate([mask_float, jnp.zeros_like(mask_float)], axis=1)
    stacked = jnp.concatenate([stacked, mask_row[None]], axis=0)
    share = stacked.reshape((F + 1) * owned, 2 * W)
    pieces = lax.all_gather(share, "col", axis=0, tiled=True)
    pieces = pieces.reshape(columns, F + 1, owned, 2 * W)
    gathered_mask = pieces[:, F, :, :W].reshape(columns * owned, W)
    left_all = pieces.transpose(1, 0, 2, 3).reshape(F + 1, columns * owned, 2 * W)
    rows = lax.axis_size("row")
    copies = jnp.broadcast_to(stacked[None], (rows,) + stacked.shape)
    got = lax.all_to_all(copies, "row", split_axis=0, concat_axis=0, tiled=True)
    right_all = got.transpose(1, 0, 2, 3).reshape(F + 1, rows * owned, 2 * W)
    left, left_mask = left_all[:F], gathered_mask
    right, right_mask = right_all[:F], right_all[F, :, :W]
    counts = jnp.dot(left_mask, right_mask.T, preferred_element_type=jnp.float32)
    inverse = 1.0 / jnp.maximum(counts, 1.0)
    lane = jnp.arange(2 * W, dtype=jnp.int32)
    swap = jnp.where(
        lane[:, None] == (lane[None, :] + W) % (2 * W),
        jnp.where(lane[None, :] < W, 1.0, -1.0),
        0.0,
    ).astype(jnp.bfloat16)
    turned = jnp.einsum("fjw,wv->fjv", right, swap, preferred_element_type=jnp.float32).astype(
        jnp.bfloat16
    )
    real = jnp.einsum("fiw,fjw->ijf", left, right, preferred_element_type=jnp.float32)
    imag = jnp.einsum("fiw,fjw->ijf", left, turned, preferred_element_type=jnp.float32)
    real_part = (real * inverse[:, :, None]).astype(jnp.bfloat16)
    imag_part = (imag * inverse[:, :, None]).astype(jnp.bfloat16)
    return (real_part, imag_part)


def solution(mesh):
    placed = (
        P(("row", "col"), None, None),
        P(("row", "col")),
        P(("row", "col")),
        P(("row", "col"), None),
    )
    return jax.shard_map(
        per_device,
        mesh=mesh,
        in_specs=placed,
        out_specs=(P("row", "col", None), P("row", "col", None)),
        check_vma=False,
    )
```

```python
import math

import jax
import jax.numpy as jnp
from jax import lax
from jax.sharding import PartitionSpec as P

F = 384
L = 3072
F0 = 13
BAND = 64
CAP = 2
W = 64


def transform_table():
    freqs = jnp.arange(F, dtype=jnp.int32) + F0
    high = jnp.arange(L // 64, dtype=jnp.int32)[:, None] * 64 * freqs[None, :] % L
    low = jnp.arange(64, dtype=jnp.int32)[:, None] * freqs[None, :] % L
    scale = 2.0 * math.pi / L
    ah = high.astype(jnp.float32) * scale
    al = low.astype(jnp.float32) * scale
    ch, sh = jnp.cos(ah)[:, None, :], jnp.sin(ah)[:, None, :]
    cl, sl = jnp.cos(al)[None, :, :], jnp.sin(al)[None, :, :]
    cos_part = (ch * cl - sh * sl).reshape(L, F)
    sin_part = (sh * cl + ch * sl).reshape(L, F)
    return jnp.concatenate([cos_part, -sin_part], axis=1).astype(jnp.bfloat16)


def whiten(segments, table):
    count = segments.shape[0]
    spectrum = jnp.dot(segments.reshape(count * W, L), table, preferred_element_type=jnp.float32)
    real = spectrum[:, :F]
    imag = spectrum[:, F:]
    power = (real * real + imag * imag).reshape(count * W, F // BAND, BAND)
    factor = lax.rsqrt(jnp.mean(power, axis=2) + 1e-05)
    factor = jnp.tile(jnp.repeat(factor, BAND, axis=1), (1, 2))
    white = spectrum * factor
    return white.astype(jnp.bfloat16).reshape(count, W, 2 * F)


def per_device(recorded, seg_count, slot_station, window_mask):
    columns = lax.axis_size("col")
    slots_here = recorded.shape[0]
    owned = window_mask.shape[0]
    outgoing = columns * CAP
    slot_index = jnp.arange(slots_here, dtype=jnp.int32)
    live = slot_index < seg_count[0]
    target_col = jnp.where(live, slot_station // owned % columns, columns)
    onehot = (target_col[:, None] == jnp.arange(columns, dtype=jnp.int32)[None, :]).astype(
        jnp.int32
    )
    earlier = jnp.cumsum(onehot, axis=0) - onehot
    rank = jnp.sum(earlier * onehot, axis=1)
    position = jnp.where(live, target_col * CAP + rank, outgoing)
    chosen = position[None, :] == jnp.arange(outgoing, dtype=jnp.int32)[:, None]
    source = jnp.sum(jnp.where(chosen, slot_index[None, :], 0), axis=1)
    local_id = jnp.sum(jnp.where(chosen, slot_station[None, :] % owned + 1, 0), axis=1) - 1
    labels = local_id.astype(jnp.bfloat16).reshape(columns, CAP)
    table = transform_table()
    local_white = whiten(recorded, table)
    payload = jnp.take(local_white, source, axis=0).reshape(columns, CAP * W, 2 * F)
    label_rows = jnp.zeros((columns, 8, 2 * F), jnp.bfloat16).at[:, 0, :CAP].set(labels)
    payload = jnp.concatenate([payload, label_rows], axis=1)
    arrived = lax.all_to_all(payload, "col", split_axis=0, concat_axis=0, tiled=True)
    tags = arrived[:, CAP * W, :CAP].reshape(outgoing).astype(jnp.int32)
    match = tags[None, :] == jnp.arange(owned, dtype=jnp.int32)[:, None]
    pick = jnp.sum(jnp.where(match, jnp.arange(outgoing, dtype=jnp.int32)[None, :], 0), axis=1)
    block_rows = arrived.shape[1]
    first_row = pick // CAP * block_rows + pick % CAP * W
    row_index = first_row[:, None] + jnp.arange(W, dtype=jnp.int32)[None, :]
    spectra = jnp.take(arrived.reshape(columns * block_rows, 2 * F), row_index, axis=0)
    mask_float = window_mask.astype(jnp.bfloat16)
    spectra = spectra * mask_float[:, :, None]
    stacked = spectra.reshape(owned, W, 2, F).transpose(3, 0, 2, 1).reshape(F, owned, 2 * W)
    mask_row = jnp.concatenate([mask_float, jnp.zeros_like(mask_float)], axis=1)
    stacked = jnp.concatenate([stacked, mask_row[None]], axis=0)
    share = stacked.reshape((F + 1) * owned, 2 * W)
    pieces = lax.all_gather(share, "col", axis=0, tiled=True)
    pieces = pieces.reshape(columns, F + 1, owned, 2 * W)
    gathered_mask = pieces[:, F, :, :W].reshape(columns * owned, W)
    left_all = pieces.transpose(1, 0, 2, 3).reshape(F + 1, columns * owned, 2 * W)
    rows = lax.axis_size("row")
    copies = jnp.broadcast_to(stacked[None], (rows,) + stacked.shape)
    got = lax.all_to_all(copies, "row", split_axis=0, concat_axis=0, tiled=True)
    right_all = got.transpose(1, 0, 2, 3).reshape(F + 1, rows * owned, 2 * W)
    left, left_mask = left_all[:F], gathered_mask
    right, right_mask = right_all[:F], right_all[F, :, :W]
    counts = jnp.dot(left_mask, right_mask.T, preferred_element_type=jnp.float32)
    inverse = 1.0 / jnp.maximum(counts, 1.0)
    lane = jnp.arange(2 * W, dtype=jnp.int32)
    swap = jnp.where(
        lane[:, None] == (lane[None, :] + W) % (2 * W),
        jnp.where(lane[None, :] < W, 1.0, -1.0),
        0.0,
    ).astype(jnp.bfloat16)
    turned = jnp.einsum("fjw,wv->fjv", right, swap, preferred_element_type=jnp.float32).astype(
        jnp.bfloat16
    )
    real = jnp.einsum("fiw,fjw->ijf", left, right, preferred_element_type=jnp.float32)
    imag = jnp.einsum("fiw,fjw->ijf", left, turned, preferred_element_type=jnp.float32)
    real_part = (real * inverse[:, :, None]).astype(jnp.bfloat16)
    imag_part = (imag * inverse[:, :, None]).astype(jnp.bfloat16)
    return (real_part, imag_part)


def solution(mesh):
    placed = (
        P(("row", "col"), None, None),
        P(("row", "col")),
        P(("row", "col")),
        P(("row", "col"), None),
    )
    return jax.shard_map(
        per_device,
        mesh=mesh,
        in_specs=placed,
        out_specs=(P("row", "col", None), P("row", "col", None)),
        check_vma=False,
    )
```

```python
import math

import jax
import jax.numpy as jnp
from jax import lax
from jax.sharding import PartitionSpec as P

F = 384
L = 3072
F0 = 13
BAND = 64
CAP = 2
W = 64


def transform_table():
    freqs = jnp.arange(F, dtype=jnp.int32) + F0
    high = jnp.arange(L // 64, dtype=jnp.int32)[:, None] * 64 * freqs[None, :] % L
    low = jnp.arange(64, dtype=jnp.int32)[:, None] * freqs[None, :] % L
    scale = 2.0 * math.pi / L
    ah = high.astype(jnp.float32) * scale
    al = low.astype(jnp.float32) * scale
    ch, sh = jnp.cos(ah)[:, None, :], jnp.sin(ah)[:, None, :]
    cl, sl = jnp.cos(al)[None, :, :], jnp.sin(al)[None, :, :]
    cos_part = (ch * cl - sh * sl).reshape(L, F)
    sin_part = (sh * cl + ch * sl).reshape(L, F)
    return jnp.concatenate([cos_part, -sin_part], axis=1).astype(jnp.bfloat16)


def whiten(segments, table):
    count = segments.shape[0]
    spectrum = jnp.dot(segments.reshape(count * W, L), table, preferred_element_type=jnp.float32)
    real = spectrum[:, :F]
    imag = spectrum[:, F:]
    power = (real * real + imag * imag).reshape(count * W, F // BAND, BAND)
    factor = lax.rsqrt(jnp.mean(power, axis=2) + 1e-05)
    factor = jnp.repeat(factor, BAND, axis=1)
    white = jnp.concatenate([real * factor, imag * factor], axis=1)
    return white.astype(jnp.bfloat16).reshape(count, W, 2 * F)


def per_device(recorded, seg_count, slot_station, window_mask):
    columns = lax.axis_size("col")
    slots_here = recorded.shape[0]
    owned = window_mask.shape[0]
    outgoing = columns * CAP
    slot_index = jnp.arange(slots_here, dtype=jnp.int32)
    live = slot_index < seg_count[0]
    target_col = jnp.where(live, slot_station // owned % columns, columns)
    onehot = (target_col[:, None] == jnp.arange(columns, dtype=jnp.int32)[None, :]).astype(
        jnp.int32
    )
    earlier = jnp.cumsum(onehot, axis=0) - onehot
    rank = jnp.sum(earlier * onehot, axis=1)
    position = jnp.where(live, target_col * CAP + rank, outgoing)
    chosen = position[None, :] == jnp.arange(outgoing, dtype=jnp.int32)[:, None]
    source = jnp.sum(jnp.where(chosen, slot_index[None, :], 0), axis=1)
    local_id = jnp.sum(jnp.where(chosen, slot_station[None, :] % owned + 1, 0), axis=1) - 1
    labels = local_id.astype(jnp.bfloat16).reshape(columns, CAP)
    table = transform_table()
    local_white = whiten(recorded, table)
    payload = jnp.take(local_white, source, axis=0).reshape(columns, CAP * W, 2 * F)
    label_rows = jnp.zeros((columns, 8, 2 * F), jnp.bfloat16).at[:, 0, :CAP].set(labels)
    payload = jnp.concatenate([payload, label_rows], axis=1)
    arrived = lax.all_to_all(payload, "col", split_axis=0, concat_axis=0, tiled=True)
    tags = arrived[:, CAP * W, :CAP].reshape(outgoing).astype(jnp.int32)
    flat = arrived[:, : CAP * W, :].reshape(outgoing, W, 2 * F)
    match = tags[None, :] == jnp.arange(owned, dtype=jnp.int32)[:, None]
    pick = jnp.sum(jnp.where(match, jnp.arange(outgoing, dtype=jnp.int32)[None, :], 0), axis=1)
    spectra = jnp.take(flat, pick, axis=0)
    mask_float = window_mask.astype(jnp.bfloat16)
    spectra = spectra * mask_float[:, :, None]
    stacked = spectra.reshape(owned, W, 2, F).transpose(3, 0, 2, 1).reshape(F, owned, 2 * W)
    mask_row = jnp.concatenate([mask_float, jnp.zeros_like(mask_float)], axis=1)
    stacked = jnp.concatenate([stacked, mask_row[None]], axis=0)
    share = stacked.reshape((F + 1) * owned, 2 * W)
    pieces = lax.all_gather(share, "col", axis=0, tiled=True)
    pieces = pieces.reshape(columns, F + 1, owned, 2 * W)
    gathered_mask = pieces[:, F, :, :W].reshape(columns * owned, W)
    left_all = pieces.transpose(1, 0, 2, 3).reshape(F + 1, columns * owned, 2 * W)
    rows = lax.axis_size("row")
    copies = jnp.broadcast_to(stacked[None], (rows,) + stacked.shape)
    got = lax.all_to_all(copies, "row", split_axis=0, concat_axis=0, tiled=True)
    right_all = got.transpose(1, 0, 2, 3).reshape(F + 1, rows * owned, 2 * W)
    left, left_mask = left_all[:F], gathered_mask
    right, right_mask = right_all[:F], right_all[F, :, :W]
    counts = jnp.dot(left_mask, right_mask.T, preferred_element_type=jnp.float32)
    inverse = 1.0 / jnp.maximum(counts, 1.0)
    lane = jnp.arange(2 * W, dtype=jnp.int32)
    swap = jnp.where(
        lane[:, None] == (lane[None, :] + W) % (2 * W),
        jnp.where(lane[None, :] < W, 1.0, -1.0),
        0.0,
    ).astype(jnp.bfloat16)
    turned = jnp.einsum("fjw,wv->fjv", right, swap, preferred_element_type=jnp.float32).astype(
        jnp.bfloat16
    )
    turned = lax.optimization_barrier(turned)
    real = jnp.einsum("fiw,fjw->ijf", left, right, preferred_element_type=jnp.float32)
    imag = jnp.einsum("fiw,fjw->ijf", left, turned, preferred_element_type=jnp.float32)
    real_part = (real * inverse[:, :, None]).astype(jnp.bfloat16)
    imag_part = (imag * inverse[:, :, None]).astype(jnp.bfloat16)
    return (real_part, imag_part)


def solution(mesh):
    placed = (
        P(("row", "col"), None, None),
        P(("row", "col")),
        P(("row", "col")),
        P(("row", "col"), None),
    )
    return jax.shard_map(
        per_device,
        mesh=mesh,
        in_specs=placed,
        out_specs=(P("row", "col", None), P("row", "col", None)),
        check_vma=False,
    )
```

```python
import math

import jax
import jax.numpy as jnp
from jax import lax
from jax.experimental.layout import Layout, with_layout_constraint
from jax.sharding import PartitionSpec as P

F = 384
L = 3072
F0 = 13
BAND = 64
CAP = 2
W = 64


def transform_table():
    freqs = jnp.arange(F, dtype=jnp.int32) + F0
    high = jnp.arange(L // 64, dtype=jnp.int32)[:, None] * 64 * freqs[None, :] % L
    low = jnp.arange(64, dtype=jnp.int32)[:, None] * freqs[None, :] % L
    scale = 2.0 * math.pi / L
    ah = high.astype(jnp.float32) * scale
    al = low.astype(jnp.float32) * scale
    ch, sh = jnp.cos(ah)[:, None, :], jnp.sin(ah)[:, None, :]
    cl, sl = jnp.cos(al)[None, :, :], jnp.sin(al)[None, :, :]
    cos_part = (ch * cl - sh * sl).reshape(L, F)
    sin_part = (sh * cl + ch * sl).reshape(L, F)
    return jnp.concatenate([cos_part, -sin_part], axis=1).astype(jnp.bfloat16)


def whiten(segments, table):
    count = segments.shape[0]
    spectrum = jnp.dot(segments.reshape(count * W, L), table, preferred_element_type=jnp.float32)
    real = spectrum[:, :F]
    imag = spectrum[:, F:]
    power = (real * real + imag * imag).reshape(count * W, F // BAND, BAND)
    factor = lax.rsqrt(jnp.mean(power, axis=2) + 1e-05)
    factor = jnp.repeat(factor, BAND, axis=1)
    white = jnp.concatenate([real * factor, imag * factor], axis=1)
    return white.astype(jnp.bfloat16).reshape(count, W, 2 * F)


def per_device(recorded, seg_count, slot_station, window_mask):
    columns = lax.axis_size("col")
    slots_here = recorded.shape[0]
    owned = window_mask.shape[0]
    outgoing = columns * CAP
    slot_index = jnp.arange(slots_here, dtype=jnp.int32)
    live = slot_index < seg_count[0]
    target_col = jnp.where(live, slot_station // owned % columns, columns)
    onehot = (target_col[:, None] == jnp.arange(columns, dtype=jnp.int32)[None, :]).astype(
        jnp.int32
    )
    earlier = jnp.cumsum(onehot, axis=0) - onehot
    rank = jnp.sum(earlier * onehot, axis=1)
    position = jnp.where(live, target_col * CAP + rank, outgoing)
    chosen = position[None, :] == jnp.arange(outgoing, dtype=jnp.int32)[:, None]
    source = jnp.sum(jnp.where(chosen, slot_index[None, :], 0), axis=1)
    local_id = jnp.sum(jnp.where(chosen, slot_station[None, :] % owned + 1, 0), axis=1) - 1
    labels = local_id.astype(jnp.bfloat16).reshape(columns, CAP)
    table = transform_table()
    local_white = whiten(recorded, table)
    payload = jnp.take(local_white, source, axis=0).reshape(columns, CAP * W, 2 * F)
    label_rows = jnp.zeros((columns, 8, 2 * F), jnp.bfloat16).at[:, 0, :CAP].set(labels)
    payload = jnp.concatenate([payload, label_rows], axis=1)
    arrived = lax.all_to_all(payload, "col", split_axis=0, concat_axis=0, tiled=True)
    tags = arrived[:, CAP * W, :CAP].reshape(outgoing).astype(jnp.int32)
    flat = arrived[:, : CAP * W, :].reshape(outgoing, W, 2 * F)
    match = tags[None, :] == jnp.arange(owned, dtype=jnp.int32)[:, None]
    pick = jnp.sum(jnp.where(match, jnp.arange(outgoing, dtype=jnp.int32)[None, :], 0), axis=1)
    spectra = jnp.take(flat, pick, axis=0)
    mask_float = window_mask.astype(jnp.bfloat16)
    spectra = spectra * mask_float[:, :, None]
    stacked = spectra.reshape(owned, W, 2, F).transpose(3, 0, 2, 1).reshape(F, owned, 2 * W)
    mask_row = jnp.concatenate([mask_float, jnp.zeros_like(mask_float)], axis=1)
    stacked = jnp.concatenate([stacked, mask_row[None]], axis=0)
    share = stacked.reshape((F + 1) * owned, 2 * W)
    pieces = lax.all_gather(share, "col", axis=0, tiled=True)
    pieces = pieces.reshape(columns, F + 1, owned, 2 * W)
    gathered_mask = pieces[:, F, :, :W].reshape(columns * owned, W)
    left_all = pieces.transpose(1, 0, 2, 3).reshape(F + 1, columns * owned, 2 * W)
    rows = lax.axis_size("row")
    copies = jnp.broadcast_to(stacked[None], (rows,) + stacked.shape)
    got = lax.all_to_all(copies, "row", split_axis=0, concat_axis=0, tiled=True)
    right_all = got.transpose(1, 0, 2, 3).reshape(F + 1, rows * owned, 2 * W)
    left, left_mask = left_all[:F], gathered_mask
    right, right_mask = right_all[:F], right_all[F, :, :W]
    counts = jnp.dot(left_mask, right_mask.T, preferred_element_type=jnp.float32)
    inverse = 1.0 / jnp.maximum(counts, 1.0)
    lane = jnp.arange(2 * W, dtype=jnp.int32)
    swap = jnp.where(
        lane[:, None] == (lane[None, :] + W) % (2 * W),
        jnp.where(lane[None, :] < W, 1.0, -1.0),
        0.0,
    ).astype(jnp.bfloat16)
    turned = jnp.einsum("fjw,wv->fjv", right, swap, preferred_element_type=jnp.float32).astype(
        jnp.bfloat16
    )
    across = right.shape[1]
    both = jnp.concatenate([right, turned], axis=1)
    product = jnp.einsum("fiw,fjw->fij", left, both, preferred_element_type=jnp.float32)
    scale = jnp.concatenate([inverse, inverse], axis=1)
    product = (product * scale[None]).astype(jnp.bfloat16)
    product = with_layout_constraint(product, Layout((0, 1, 2)))
    return (product[:, :, :across].transpose(1, 2, 0), product[:, :, across:].transpose(1, 2, 0))


def solution(mesh):
    placed = (
        P(("row", "col"), None, None),
        P(("row", "col")),
        P(("row", "col")),
        P(("row", "col"), None),
    )
    return jax.shard_map(
        per_device,
        mesh=mesh,
        in_specs=placed,
        out_specs=(P("row", "col", None), P("row", "col", None)),
        check_vma=False,
    )
```

```python
import math

import jax
import jax.numpy as jnp
from jax import lax
from jax.sharding import PartitionSpec as P

F = 384
L = 3072
F0 = 13
BAND = 64
CAP = 2
W = 64


def transform_table():
    freqs = jnp.arange(F, dtype=jnp.int32) + F0
    high = jnp.arange(L // 64, dtype=jnp.int32)[:, None] * 64 * freqs[None, :] % L
    low = jnp.arange(64, dtype=jnp.int32)[:, None] * freqs[None, :] % L
    scale = 2.0 * math.pi / L
    ah = high.astype(jnp.float32) * scale
    al = low.astype(jnp.float32) * scale
    ch, sh = jnp.cos(ah)[:, None, :], jnp.sin(ah)[:, None, :]
    cl, sl = jnp.cos(al)[None, :, :], jnp.sin(al)[None, :, :]
    cos_part = (ch * cl - sh * sl).reshape(L, F)
    sin_part = (sh * cl + ch * sl).reshape(L, F)
    return jnp.concatenate([cos_part, -sin_part], axis=1).astype(jnp.bfloat16)


def whiten(segments, table):
    count = segments.shape[0]
    spectrum = jnp.dot(segments.reshape(count * W, L), table, preferred_element_type=jnp.float32)
    real = spectrum[:, :F]
    imag = spectrum[:, F:]
    power = (real * real + imag * imag).reshape(count * W, F // BAND, BAND)
    factor = lax.rsqrt(jnp.mean(power, axis=2) + 1e-05)
    factor = jnp.tile(jnp.repeat(factor, BAND, axis=1), (1, 2))
    white = spectrum * factor
    return white.astype(jnp.bfloat16).reshape(count, W, 2 * F)


def per_device(recorded, seg_count, slot_station, window_mask):
    columns = lax.axis_size("col")
    slots_here = recorded.shape[0]
    owned = window_mask.shape[0]
    outgoing = columns * CAP
    slot_index = jnp.arange(slots_here, dtype=jnp.int32)
    live = slot_index < seg_count[0]
    target_col = jnp.where(live, slot_station // owned % columns, columns)
    onehot = (target_col[:, None] == jnp.arange(columns, dtype=jnp.int32)[None, :]).astype(
        jnp.int32
    )
    earlier = jnp.cumsum(onehot, axis=0) - onehot
    rank = jnp.sum(earlier * onehot, axis=1)
    position = jnp.where(live, target_col * CAP + rank, outgoing)
    chosen = position[None, :] == jnp.arange(outgoing, dtype=jnp.int32)[:, None]
    source = jnp.sum(jnp.where(chosen, slot_index[None, :], 0), axis=1)
    local_id = jnp.sum(jnp.where(chosen, slot_station[None, :] % owned + 1, 0), axis=1) - 1
    labels = local_id.astype(jnp.bfloat16).reshape(columns, CAP)
    table = transform_table()
    local_white = whiten(recorded, table)
    payload = jnp.take(local_white, source, axis=0).reshape(columns, CAP * W, 2 * F)
    label_rows = jnp.zeros((columns, 8, 2 * F), jnp.bfloat16).at[:, 0, :CAP].set(labels)
    payload = jnp.concatenate([payload, label_rows], axis=1)
    arrived = lax.all_to_all(payload, "col", split_axis=0, concat_axis=0, tiled=True)
    tags = arrived[:, CAP * W, :CAP].reshape(outgoing).astype(jnp.int32)
    match = tags[None, :] == jnp.arange(owned, dtype=jnp.int32)[:, None]
    pick = jnp.sum(jnp.where(match, jnp.arange(outgoing, dtype=jnp.int32)[None, :], 0), axis=1)
    block_rows = arrived.shape[1]
    first_row = pick // CAP * block_rows + pick % CAP * W
    row_index = first_row[:, None] + jnp.arange(W, dtype=jnp.int32)[None, :]
    spectra = jnp.take(arrived.reshape(columns * block_rows, 2 * F), row_index, axis=0)
    mask_float = window_mask.astype(jnp.bfloat16)
    spectra = spectra * mask_float[:, :, None]
    stacked = spectra.reshape(owned, W, 2, F).transpose(3, 0, 2, 1).reshape(F, owned, 2 * W)
    mask_row = jnp.concatenate([mask_float, jnp.zeros_like(mask_float)], axis=1)
    stacked = jnp.concatenate([stacked, mask_row[None]], axis=0)
    share = stacked.reshape((F + 1) * owned, 2 * W)
    pieces = lax.all_gather(share, "col", axis=0, tiled=True)
    pieces = pieces.reshape(columns, F + 1, owned, 2 * W)
    gathered_mask = pieces[:, F, :, :W].reshape(columns * owned, W)
    left_all = pieces.transpose(1, 0, 2, 3).reshape(F + 1, columns * owned, 2 * W)
    rows = lax.axis_size("row")
    copies = jnp.broadcast_to(stacked[None], (rows,) + stacked.shape)
    got = lax.all_to_all(copies, "row", split_axis=0, concat_axis=0, tiled=True)
    right_all = got.transpose(1, 0, 2, 3).reshape(F + 1, rows * owned, 2 * W)
    left, left_mask = left_all[:F], gathered_mask
    right, right_mask = right_all[:F], right_all[F, :, :W]
    counts = jnp.dot(left_mask, right_mask.T, preferred_element_type=jnp.float32)
    inverse = 1.0 / jnp.maximum(counts, 1.0)
    lane = jnp.arange(2 * W, dtype=jnp.int32)
    swap = jnp.where(
        lane[:, None] == (lane[None, :] + W) % (2 * W),
        jnp.where(lane[None, :] < W, 1.0, -1.0),
        0.0,
    ).astype(jnp.bfloat16)
    turned = jnp.einsum("fjw,wv->fjv", right, swap, preferred_element_type=jnp.float32).astype(
        jnp.bfloat16
    )
    turned = lax.optimization_barrier(turned)
    real = jnp.einsum("fiw,fjw->ijf", left, right, preferred_element_type=jnp.float32)
    imag = jnp.einsum("fiw,fjw->ijf", left, turned, preferred_element_type=jnp.float32)
    real_part = (real * inverse[:, :, None]).astype(jnp.bfloat16)
    imag_part = (imag * inverse[:, :, None]).astype(jnp.bfloat16)
    return (real_part, imag_part)


def solution(mesh):
    placed = (
        P(("row", "col"), None, None),
        P(("row", "col")),
        P(("row", "col")),
        P(("row", "col"), None),
    )
    return jax.shard_map(
        per_device,
        mesh=mesh,
        in_specs=placed,
        out_specs=(P("row", "col", None), P("row", "col", None)),
        check_vma=False,
    )
```
